1024 devices in a mesh: tm: 256 (over z, y, core), space: 4 (over x).
Axes of the slice: x: 4, y: 8, z: 16, core: 2. Of those that a mesh axis runs over, the one named last changes fastest.
Arguments:
- video: bfloat16 [512, 32, 64, 128], P('tm', 'space'), may hold values from -6 to 6
- w_space: bfloat16 [3, 3, 128, 128], replicated, may hold values from -0.1875 to 0.1875
- w_time: bfloat16 [3, 128, 128], replicated, may hold values from -0.3125 to 0.3125
- w_merge1: bfloat16 [2, 128, 128], replicated, may hold values from -0.375 to 0.375
- w_merge2: bfloat16 [2, 128, 128], replicated, may hold values from -0.375 to 0.375
- cotangent: bfloat16 [256, 32, 64, 64], P('tm', 'space'), may hold values from -6 to 6
Outputs:
- conv_grad: bfloat16 [512, 32, 64, 128], P('tm', 'space')
- space_grad: float32 [147456], P(('tm', 'space'))
The draws below stay inside these ranges and needn't reach their ends.
All inputs are finite; a program needn't handle non-finite values.
Results may differ from the reference program's by a relative error of at most 0.0061.
Values may be sent and summed in bfloat16 or wider, within the bound.
No kernel may reach another device: no remote copies, remote signals or barrier semaphores. Data moves between devices by JAX's collectives and lax.ppermute only.
A program may use at most 32 MiB of HBM per device.

```python
import math
import jax
import jax.numpy as jnp
from jax import lax

C = 128
W = 64
FRAMES = 512
H = 32


def block_scale(own_key, extent, cuts, least, high):
    gain = 1.0
    for dim, shards_of in cuts:
        steps = jax.random.uniform(jax.random.fold_in(jax.random.fold_in(own_key, 6), dim), (shards_of,), jnp.float32, least / len(cuts), high / len(cuts))
        gain = gain * jnp.repeat(jnp.exp(steps), extent[dim] // shards_of).reshape((-1,) + (1,) * (len(extent) - 1 - dim))
    return gain


def bell_draw(key, shape, spread, bound, cuts=(), kind=jnp.bfloat16):
    values = jax.random.normal(key, shape, jnp.float32) * spread
    if len(cuts) > 0:
        values = block_scale(key, shape, cuts, -0.22, 0.18) * values
    return jnp.clip(values, min=-bound, max=bound).astype(kind)


def setup_inputs(seed: int = 0) -> dict:
    streams_of = jax.random.split(jax.random.key(seed), 7)
    return {
        "video": bell_draw(streams_of[0], (FRAMES, H, W, C), 1.0, 6.0, ((0, 256), (1, 4))),
        "w_space": bell_draw(streams_of[1], (3, 3, C, C), (9 * C) ** -0.5, 0.1875),
        "w_time": bell_draw(streams_of[2], (3, C, C), (3 * C) ** -0.5, 0.3125),
        "w_merge1": bell_draw(streams_of[3], (2, C, C), (2 * C) ** -0.5, 0.375),
        "w_merge2": bell_draw(streams_of[4], (2, C, C), (2 * C) ** -0.5, 0.375),
        "cotangent": bell_draw(streams_of[5], (FRAMES // 2, H, W, C // 2), 1.0, 6.0, ((0, 256), (1, 4))),
    }


def project(values, weight):
    flat = values.reshape(-1, values.shape[-1])
    result = jnp.dot(flat, weight, preferred_element_type=jnp.float32)
    return result.reshape(values.shape[:-1] + (weight.shape[-1],))

def spatial_conv(padded, w_space, band_rows, band_cols):
    total = None
    for row_tap in range(3):
        for col_tap in range(3):
            window = padded[..., row_tap:row_tap + band_rows, col_tap:col_tap + band_cols, :]
            term = project(window, w_space[row_tap, col_tap])
            total = term if total is None else total + term
    return total.astype(jnp.bfloat16)

def reference(video, w_space, w_time, w_merge1, w_merge2, cotangent):
    frame_count, height, width, channels = video.shape

    def forward(carry, frame):
        padded = jnp.pad(frame, ((1, 1), (1, 1), (0, 0)))
        return (carry, spatial_conv(padded, w_space, height, width))
    _, conv = lax.scan(forward, jnp.zeros((), jnp.float32), video)
    blank = jnp.zeros((2, height, width, channels), conv.dtype)
    history = jnp.concatenate([blank, conv], axis=0)

    def backward(carry, frame_index):
        next_one, next_two, grads = carry
        three = lax.dynamic_slice_in_dim(history, frame_index, 3, 0)
        preact = project(three[2], w_time[0]) + project(three[1], w_time[1]) + project(three[0], w_time[2])
        level_index = frame_index // 2
        merged_index = frame_index // 4
        couple = lax.dynamic_slice_in_dim(cotangent, (2 * merged_index).astype(jnp.int32), 2, 0)
        full_grad = jnp.concatenate([couple[0], couple[1]], axis=-1)
        level_weight = lax.dynamic_index_in_dim(w_merge2, level_index % 2, 0, keepdims=False)
        level_grad = project(full_grad, level_weight.T).astype(jnp.bfloat16)
        first_weight = lax.dynamic_index_in_dim(w_merge1, frame_index % 2, 0, keepdims=False)
        hidden_grad = project(level_grad, first_weight.T)
        sigmoid_a = jax.nn.sigmoid(preact)
        slope = sigmoid_a * (1.0 + preact * (1.0 - sigmoid_a))
        act_grad = (hidden_grad * slope).astype(jnp.bfloat16)
        conv_sum = project(act_grad, w_time[0].T) + project(next_one, w_time[1].T) + project(next_two, w_time[2].T)
        conv_grad = conv_sum.astype(jnp.bfloat16)
        frame = lax.dynamic_index_in_dim(video, frame_index, 0, keepdims=False)
        padded = jnp.pad(frame, ((1, 1), (1, 1), (0, 0)))
        flat_grad = conv_grad.reshape(-1, channels)
        taps = []
        for row_tap in range(3):
            for col_tap in range(3):
                window = padded[row_tap:row_tap + height, col_tap:col_tap + width, :].reshape(-1, channels)
                taps.append(jnp.dot(window.T, flat_grad, preferred_element_type=jnp.float32))
        grads = grads + jnp.stack(taps).reshape(3, 3, channels, channels)
        return ((act_grad, next_one, grads), conv_grad)
    empty_frame = jnp.zeros((height, width, channels), jnp.bfloat16)
    start = (empty_frame, empty_frame, jnp.zeros((3, 3, channels, channels), jnp.float32))
    order = jnp.arange(frame_count - 1, -1, -1, dtype=jnp.int32)
    (_, _, grads), reversed_grad = lax.scan(backward, start, order)
    scale = 1.0 / math.sqrt(frame_count * height * width)
    return (reversed_grad[::-1], (grads * scale).reshape(-1))
```

```python
import math

import jax
import jax.numpy as jnp
from jax import lax
from jax.sharding import PartitionSpec as P


def swapped(value, axis, bit):
    mask = 2**bit
    pairs = [(source, source ^ mask) for source in range(lax.axis_size(axis))]
    return lax.ppermute(value, axis, pairs)


def with_halo(block, sides, width):
    for axis, dim in sides:
        count = lax.axis_size(axis)
        forward = [(i, i + 1) for i in range(count - 1)]
        backward = [(target, source) for source, target in forward]
        low = lax.ppermute(
            lax.slice_in_dim(block, block.shape[dim] - width, None, axis=dim), axis, forward
        )
        high = lax.ppermute(lax.slice_in_dim(block, 0, width, axis=dim), axis, backward)
        block = jnp.concatenate([low, block, high], axis=dim)
    return block


def shifted(value, axis, steps):
    count = lax.axis_size(axis)
    first, last = (max(0, -steps), min(count, count - steps))
    return lax.ppermute(value, axis, [(source, source + steps) for source in range(first, last)])


def project(values, weight):
    flat = values.reshape(-1, values.shape[-1])
    result = jnp.dot(flat, weight, preferred_element_type=jnp.float32)
    return result.reshape(values.shape[:-1] + (weight.shape[-1],))


def spatial_conv(padded, w_space, band_rows, band_cols):
    total = None
    for row_tap in range(3):
        for col_tap in range(3):
            window = padded[..., row_tap : row_tap + band_rows, col_tap : col_tap + band_cols, :]
            term = project(window, w_space[row_tap, col_tap])
            total = term if total is None else total + term
    return total.astype(jnp.bfloat16)


def halving_sum(local_grad):
    position = lax.axis_index(("tm", "space"))
    levels = lax.axis_size(("tm", "space")).bit_length() - 1
    holding = local_grad
    for bit in reversed(range(levels)):
        half_len = holding.shape[0] // 2
        lower = holding[:half_len]
        upper = holding[half_len:]
        upper_side = position >> bit & 1 == 1
        keeping = jnp.where(upper_side, upper, lower)
        sending = jnp.where(upper_side, lower, upper)
        holding = keeping + swapped(sending, ("tm", "space"), bit)
    return holding


def per_device(video, w_space, w_time, w_merge1, w_merge2, cotangent):
    band_rows = video.shape[1]
    band_cols = video.shape[2]
    channels = video.shape[3]
    with_rows = with_halo(video, (("space", 1),), 1)
    padded = jnp.pad(with_rows, ((0, 0), (0, 0), (1, 1), (0, 0)))
    conv = spatial_conv(padded, w_space, band_rows, band_cols)
    earlier = shifted(conv, "tm", 1)
    history = jnp.concatenate([earlier, conv], axis=0)
    preact = (
        project(history[2:4], w_time[0])
        + project(history[1:3], w_time[1])
        + project(history[0:2], w_time[2])
    )
    parity = lax.axis_index("tm") % 2
    own_half = cotangent[0]
    level_weight = lax.dynamic_index_in_dim(w_merge2, parity, 0, keepdims=False)
    partner_half = swapped(cotangent, "tm", 0)[0]
    leading = jnp.where(parity == 0, own_half, partner_half)
    trailing = jnp.where(parity == 0, partner_half, own_half)
    full_grad = jnp.concatenate([leading, trailing], axis=-1)
    level_sum = project(full_grad, level_weight.T)
    level_grad = level_sum.astype(jnp.bfloat16)
    hidden_grad = jnp.stack(
        [project(level_grad, w_merge1[0].T), project(level_grad, w_merge1[1].T)]
    )
    sigmoid_a = jax.nn.sigmoid(preact)
    slope = sigmoid_a * (1.0 + preact * (1.0 - sigmoid_a))
    act_grad = (hidden_grad * slope).astype(jnp.bfloat16)
    later = shifted(act_grad, "tm", -1)
    future = jnp.concatenate([act_grad, later], axis=0)
    conv_sum = (
        project(future[0:2], w_time[0].T)
        + project(future[1:3], w_time[1].T)
        + project(future[2:4], w_time[2].T)
    )
    conv_grad = conv_sum.astype(jnp.bfloat16)
    flat_grad = conv_grad.reshape(-1, channels)
    taps = []
    for row_tap in range(3):
        for col_tap in range(3):
            window = padded[
                :, row_tap : row_tap + band_rows, col_tap : col_tap + band_cols, :
            ].reshape(-1, channels)
            taps.append(jnp.dot(window.T, flat_grad, preferred_element_type=jnp.float32))
    local_grad = jnp.stack(taps).reshape(-1)
    summed = lax.psum_scatter(local_grad, ("tm", "space"), scatter_dimension=0, tiled=True)
    count = video.shape[0] * lax.axis_size("tm") * band_rows * lax.axis_size("space") * band_cols
    return (conv_grad, summed * (1.0 / math.sqrt(count)))


def solution(mesh):
    placed = (P("tm", "space", None, None), P(), P(), P(), P(), P("tm", "space", None, None))
    return jax.shard_map(
        per_device,
        mesh=mesh,
        in_specs=placed,
        out_specs=(P("tm", "space", None, None), P(("tm", "space"))),
        check_vma=False,
    )
```

```python
import math

import jax
import jax.numpy as jnp
from jax import lax
from jax.sharding import Mesh, PartitionSpec as P

TM = ("z", "y", "c")
SPACE = "x"
ROUNDS = ("c", "x", "y", "z")
AXES = ("z", "y", "c", "x")
MODE = "a2a"


def swapped(value, axis, bit):
    mask = 2**bit
    pairs = [(source, source ^ mask) for source in range(lax.axis_size(axis))]
    return lax.ppermute(value, axis, pairs)


def with_halo(block, sides, width):
    for axis, dim in sides:
        count = lax.axis_size(axis)
        forward = [(i, i + 1) for i in range(count - 1)]
        backward = [(target, source) for source, target in forward]
        low = lax.ppermute(
            lax.slice_in_dim(block, block.shape[dim] - width, None, axis=dim), axis, forward
        )
        high = lax.ppermute(lax.slice_in_dim(block, 0, width, axis=dim), axis, backward)
        block = jnp.concatenate([low, block, high], axis=dim)
    return block


def shifted(value, axis, steps):
    count = lax.axis_size(axis)
    first, last = (max(0, -steps), min(count, count - steps))
    return lax.ppermute(value, axis, [(source, source + steps) for source in range(first, last)])


def project(values, weight):
    flat = values.reshape(-1, values.shape[-1])
    result = jnp.dot(flat, weight, preferred_element_type=jnp.float32)
    return result.reshape(values.shape[:-1] + (weight.shape[-1],))


def spatial_conv(padded, w_space, band_rows, band_cols):
    total = None
    for row_tap in range(3):
        for col_tap in range(3):
            window = padded[..., row_tap : row_tap + band_rows, col_tap : col_tap + band_cols, :]
            term = project(window, w_space[row_tap, col_tap])
            total = term if total is None else total + term
    return total.astype(jnp.bfloat16)


def halving_sum(local_grad):
    position = lax.axis_index(("tm", "space"))
    levels = lax.axis_size(("tm", "space")).bit_length() - 1
    holding = local_grad
    for bit in reversed(range(levels)):
        half_len = holding.shape[0] // 2
        lower = holding[:half_len]
        upper = holding[half_len:]
        upper_side = position >> bit & 1 == 1
        keeping = jnp.where(upper_side, upper, lower)
        sending = jnp.where(upper_side, lower, upper)
        holding = keeping + swapped(sending, ("tm", "space"), bit)
    return holding


def radix_sum(local_grad, rounds):
    sizes = [lax.axis_size(axis) for axis in AXES]
    holding = local_grad.reshape(*sizes, -1)
    order = [AXES.index(axis) for axis in rounds]
    holding = holding.transpose(*order, len(AXES)).reshape(-1)
    for axis in rounds:
        count = lax.axis_size(axis)
        pieces = holding.reshape(count, -1)
        if MODE == "a2a":
            pieces = lax.all_to_all(pieces, axis, 0, 0, tiled=True)
            holding = pieces.sum(axis=0)
        else:
            index = lax.axis_index(axis)
            holding = lax.dynamic_index_in_dim(pieces, index, 0, keepdims=False)
            for step in range(1, count):
                chunk = lax.dynamic_index_in_dim(pieces, (index + step) % count, 0, keepdims=False)
                pairs = [(source, (source + step) % count) for source in range(count)]
                holding = holding + lax.ppermute(chunk, axis, pairs)
    return holding


def per_device(video, w_space, w_time, w_merge1, w_merge2, cotangent):
    band_rows = video.shape[1]
    band_cols = video.shape[2]
    channels = video.shape[3]
    with_rows = with_halo(video, ((SPACE, 1),), 1)
    padded = jnp.pad(with_rows, ((0, 0), (0, 0), (1, 1), (0, 0)))
    conv = spatial_conv(padded, w_space, band_rows, band_cols)
    earlier = shifted(conv, TM, 1)
    history = jnp.concatenate([earlier, conv], axis=0)
    preact = (
        project(history[2:4], w_time[0])
        + project(history[1:3], w_time[1])
        + project(history[0:2], w_time[2])
    )
    parity = lax.axis_index(TM) % 2
    own_half = cotangent[0]
    level_weight = lax.dynamic_index_in_dim(w_merge2, parity, 0, keepdims=False)
    partner_half = swapped(cotangent, TM, 0)[0]
    leading = jnp.where(parity == 0, own_half, partner_half)
    trailing = jnp.where(parity == 0, partner_half, own_half)
    full_grad = jnp.concatenate([leading, trailing], axis=-1)
    level_sum = project(full_grad, level_weight.T)
    level_grad = level_sum.astype(jnp.bfloat16)
    hidden_grad = jnp.stack(
        [project(level_grad, w_merge1[0].T), project(level_grad, w_merge1[1].T)]
    )
    sigmoid_a = jax.nn.sigmoid(preact)
    slope = sigmoid_a * (1.0 + preact * (1.0 - sigmoid_a))
    act_grad = (hidden_grad * slope).astype(jnp.bfloat16)
    later = shifted(act_grad, TM, -1)
    future = jnp.concatenate([act_grad, later], axis=0)
    conv_sum = (
        project(future[0:2], w_time[0].T)
        + project(future[1:3], w_time[1].T)
        + project(future[2:4], w_time[2].T)
    )
    conv_grad = conv_sum.astype(jnp.bfloat16)
    flat_grad = conv_grad.reshape(-1, channels)
    taps = []
    for row_tap in range(3):
        for col_tap in range(3):
            window = padded[
                :, row_tap : row_tap + band_rows, col_tap : col_tap + band_cols, :
            ].reshape(-1, channels)
            taps.append(jnp.dot(window.T, flat_grad, preferred_element_type=jnp.float32))
    local_grad = jnp.stack(taps).reshape(-1)
    summed = radix_sum(local_grad, ROUNDS)
    count = video.shape[0] * lax.axis_size(TM) * band_rows * lax.axis_size(SPACE) * band_cols
    return (conv_grad, summed * (1.0 / math.sqrt(count)))


def solution(mesh):
    tm_count, space_count = mesh.devices.shape
    grid = mesh.devices.reshape(tm_count // 16, 8, 2, space_count)
    fine = Mesh(grid, ("z", "y", "c", "x"))
    placed = (P(TM, SPACE, None, None), P(), P(), P(), P(), P(TM, SPACE, None, None))
    return jax.shard_map(
        per_device,
        mesh=fine,
        in_specs=placed,
        out_specs=(P(TM, SPACE, None, None), P(TM + (SPACE,))),
        check_vma=False,
    )
```

```python
import math

import jax
import jax.numpy as jnp
from jax import lax
from jax.sharding import Mesh, PartitionSpec as P

TM = ("z", "y", "c")
SPACE = "x"
AXES = ("z", "y", "c", "x")
ROUNDS = (("c", "x"), ("y", "z"))


def with_halo(block, sides, width):
    for axis, dim in sides:
        count = lax.axis_size(axis)
        forward = [(i, i + 1) for i in range(count - 1)]
        backward = [(target, source) for source, target in forward]
        low = lax.ppermute(
            lax.slice_in_dim(block, block.shape[dim] - width, None, axis=dim), axis, forward
        )
        high = lax.ppermute(lax.slice_in_dim(block, 0, width, axis=dim), axis, backward)
        block = jnp.concatenate([low, block, high], axis=dim)
    return block


def shifted(value, axis, steps, receivers=None):
    count = lax.axis_size(axis)
    first, last = (max(0, -steps), min(count, count - steps))
    pairs = [(source, source + steps) for source in range(first, last)]
    if receivers is not None:
        pairs = [(s, t) for s, t in pairs if receivers(t)]
    return lax.ppermute(value, axis, pairs)


def project(values, weight):
    flat = values.reshape(-1, values.shape[-1])
    result = jnp.dot(flat, weight, preferred_element_type=jnp.float32)
    return result.reshape(values.shape[:-1] + (weight.shape[-1],))


def spatial_conv(padded, w_space, band_rows, band_cols):
    total = None
    for row_tap in range(3):
        for col_tap in range(3):
            window = padded[..., row_tap : row_tap + band_rows, col_tap : col_tap + band_cols, :]
            term = project(window, w_space[row_tap, col_tap])
            total = term if total is None else total + term
    return total.astype(jnp.bfloat16)


def radix_sum(local_grad, rounds):
    sizes = [lax.axis_size(axis) for axis in AXES]
    holding = local_grad.reshape(*sizes, -1)
    order = [AXES.index(axis) for group in rounds for axis in group]
    holding = holding.transpose(*order, len(AXES)).reshape(-1)
    for axis in rounds:
        count = lax.axis_size(axis)
        pieces = holding.reshape(count, -1)
        if pieces.shape[1] % 1024 == 0:
            pieces = pieces.reshape(count, -1, 128)
        pieces = lax.all_to_all(pieces, axis, 0, 0, tiled=True)
        holding = pieces.sum(axis=0).reshape(-1)
    return holding


def merged_grad(leading, trailing, weight):
    full_grad = jnp.concatenate([leading, trailing], axis=-1)
    return project(full_grad, weight.T).astype(jnp.bfloat16)


def per_device(video, w_space, w_time, w_merge1, w_merge2, cotangent):
    frames, band_rows, band_cols, channels = video.shape
    assert frames == 2
    half = cotangent.shape[-1]
    position = lax.axis_index(TM)
    count_tm = lax.axis_size(TM)
    parity = position % 2
    flat_video = video.reshape(-1, channels)
    flat_cot = cotangent.reshape(-1, channels)
    parcel = jnp.concatenate([flat_video, flat_cot], axis=0)
    split = flat_video.shape[0]
    from_prev = shifted(parcel, TM, 1)
    from_next = shifted(parcel, TM, -1)
    cot_after_next = shifted(cotangent, TM, -2, receivers=lambda t: t % 2 == 1)[0]
    prev_video = from_prev[:split].reshape(video.shape)
    next_video = from_next[:split].reshape(video.shape)
    cot_prev = from_prev[split:].reshape(cotangent.shape)[0]
    cot_next = from_next[split:].reshape(cotangent.shape)[0]
    own_cot = cotangent[0]
    stack = jnp.concatenate([prev_video, video, next_video], axis=0)
    with_rows = with_halo(stack, ((SPACE, 1),), 1)
    padded = jnp.pad(with_rows, ((0, 0), (0, 0), (1, 1), (0, 0)))
    conv = spatial_conv(padded, w_space, band_rows, band_cols)
    own_frames = 2 * frames
    preact = (
        project(conv[2:own_frames + 2], w_time[0])
        + project(conv[1:own_frames + 1], w_time[1])
        + project(conv[0:own_frames], w_time[2])
    )
    even = parity == 0
    own_lead = jnp.where(even, own_cot, cot_prev)
    own_trail = jnp.where(even, cot_next, own_cot)
    next_lead = jnp.where(even, own_cot, cot_next)
    next_trail = jnp.where(even, cot_next, cot_after_next)
    own_level = merged_grad(
        own_lead, own_trail, lax.dynamic_index_in_dim(w_merge2, parity, 0, keepdims=False)
    )
    next_level = merged_grad(
        next_lead, next_trail, lax.dynamic_index_in_dim(w_merge2, 1 - parity, 0, keepdims=False)
    )
    hidden_grad = jnp.stack(
        [
            project(own_level, w_merge1[0].T),
            project(own_level, w_merge1[1].T),
            project(next_level, w_merge1[0].T),
            project(next_level, w_merge1[1].T),
        ]
    )
    sigmoid_a = jax.nn.sigmoid(preact)
    slope = sigmoid_a * (1.0 + preact * (1.0 - sigmoid_a))
    act_grad = (hidden_grad * slope).astype(jnp.bfloat16)
    has_next = (jnp.arange(own_frames) < frames) | (position < count_tm - 1)
    act_grad = jnp.where(has_next[:, None, None, None], act_grad, jnp.zeros_like(act_grad))
    conv_sum = (
        project(act_grad[0:frames], w_time[0].T)
        + project(act_grad[1:frames + 1], w_time[1].T)
        + project(act_grad[2:frames + 2], w_time[2].T)
    )
    conv_grad = conv_sum.astype(jnp.bfloat16)
    flat_grad = conv_grad.reshape(-1, channels)
    own_padded = padded[frames:2 * frames]
    taps = []
    for row_tap in range(3):
        for col_tap in range(3):
            window = own_padded[
                :, row_tap : row_tap + band_rows, col_tap : col_tap + band_cols, :
            ].reshape(-1, channels)
            taps.append(jnp.dot(window.T, flat_grad, preferred_element_type=jnp.float32))
    local_grad = jnp.stack(taps).reshape(-1)
    summed = radix_sum(local_grad, ROUNDS)
    count = frames * count_tm * band_rows * lax.axis_size(SPACE) * band_cols
    return (conv_grad, summed * (1.0 / math.sqrt(count)))


def solution(mesh):
    tm_count, space_count = mesh.devices.shape
    grid = mesh.devices.reshape(tm_count // 16, 8, 2, space_count)
    fine = Mesh(grid, AXES)
    placed = (P(TM, SPACE, None, None), P(), P(), P(), P(), P(TM, SPACE, None, None))
    return jax.shard_map(
        per_device,
        mesh=fine,
        in_specs=placed,
        out_specs=(P(TM, SPACE, None, None), P(TM + (SPACE,))),
        check_vma=False,
    )
```

```python
import math

import jax
import jax.numpy as jnp
from jax import lax
from jax.sharding import Mesh, PartitionSpec as P

TM = ("z", "y", "c")
SPACE = "x"
ROUNDS = (("z", "y"), ("c", "x"))
AXES = ("z", "y", "c", "x")
MODE = 'a2a'


def swapped(value, axis, bit):
    mask = 2**bit
    pairs = [(source, source ^ mask) for source in range(lax.axis_size(axis))]
    return lax.ppermute(value, axis, pairs)


def with_halo(block, sides, width):
    for axis, dim in sides:
        count = lax.axis_size(axis)
        forward = [(i, i + 1) for i in range(count - 1)]
        backward = [(target, source) for source, target in forward]
        low = lax.ppermute(
            lax.slice_in_dim(block, block.shape[dim] - width, None, axis=dim), axis, forward
        )
        high = lax.ppermute(lax.slice_in_dim(block, 0, width, axis=dim), axis, backward)
        block = jnp.concatenate([low, block, high], axis=dim)
    return block


def shifted(value, axis, steps):
    count = lax.axis_size(axis)
    first, last = (max(0, -steps), min(count, count - steps))
    return lax.ppermute(value, axis, [(source, source + steps) for source in range(first, last)])


def project(values, weight):
    flat = values.reshape(-1, values.shape[-1])
    result = jnp.dot(flat, weight, preferred_element_type=jnp.float32)
    return result.reshape(values.shape[:-1] + (weight.shape[-1],))


def spatial_conv(padded, w_space, band_rows, band_cols):
    total = None
    for row_tap in range(3):
        for col_tap in range(3):
            window = padded[..., row_tap : row_tap + band_rows, col_tap : col_tap + band_cols, :]
            term = project(window, w_space[row_tap, col_tap])
            total = term if total is None else total + term
    return total.astype(jnp.bfloat16)


def halving_sum(local_grad):
    position = lax.axis_index(("tm", "space"))
    levels = lax.axis_size(("tm", "space")).bit_length() - 1
    holding = local_grad
    for bit in reversed(range(levels)):
        half_len = holding.shape[0] // 2
        lower = holding[:half_len]
        upper = holding[half_len:]
        upper_side = position >> bit & 1 == 1
        keeping = jnp.where(upper_side, upper, lower)
        sending = jnp.where(upper_side, lower, upper)
        holding = keeping + swapped(sending, ("tm", "space"), bit)
    return holding


def radix_sum(local_grad, rounds):
    outer, inner = rounds
    inner_count = lax.axis_size(inner)
    outer_count = lax.axis_size(outer)
    holding = local_grad.reshape(outer_count, inner_count, -1)
    holding = lax.all_to_all(holding, inner, 1, 1, tiled=True).sum(axis=1)
    holding = lax.all_to_all(holding, outer, 0, 0, tiled=True).sum(axis=0)
    return holding

def per_device(video, w_space, w_time, w_merge1, w_merge2, cotangent):
    band_rows = video.shape[1]
    band_cols = video.shape[2]
    channels = video.shape[3]
    with_rows = with_halo(video, ((SPACE, 1),), 1)
    padded = jnp.pad(with_rows, ((0, 0), (0, 0), (1, 1), (0, 0)))
    conv = spatial_conv(padded, w_space, band_rows, band_cols)
    earlier = shifted(conv, TM, 1)
    history = jnp.concatenate([earlier, conv], axis=0)
    preact = (
        project(history[2:4], w_time[0])
        + project(history[1:3], w_time[1])
        + project(history[0:2], w_time[2])
    )
    parity = lax.axis_index(TM) % 2
    own_half = cotangent[0]
    level_weight = lax.dynamic_index_in_dim(w_merge2, parity, 0, keepdims=False)
    partner_half = swapped(cotangent, TM, 0)[0]
    leading = jnp.where(parity == 0, own_half, partner_half)
    trailing = jnp.where(parity == 0, partner_half, own_half)
    full_grad = jnp.concatenate([leading, trailing], axis=-1)
    level_sum = project(full_grad, level_weight.T)
    level_grad = level_sum.astype(jnp.bfloat16)
    hidden_grad = jnp.stack(
        [project(level_grad, w_merge1[0].T), project(level_grad, w_merge1[1].T)]
    )
    sigmoid_a = jax.nn.sigmoid(preact)
    slope = sigmoid_a * (1.0 + preact * (1.0 - sigmoid_a))
    act_grad = (hidden_grad * slope).astype(jnp.bfloat16)
    later = shifted(act_grad, TM, -1)
    future = jnp.concatenate([act_grad, later], axis=0)
    conv_sum = (
        project(future[0:2], w_time[0].T)
        + project(future[1:3], w_time[1].T)
        + project(future[2:4], w_time[2].T)
    )
    conv_grad = conv_sum.astype(jnp.bfloat16)
    flat_grad = conv_grad.reshape(-1, channels)
    taps = []
    for row_tap in range(3):
        for col_tap in range(3):
            window = padded[
                :, row_tap : row_tap + band_rows, col_tap : col_tap + band_cols, :
            ].reshape(-1, channels)
            taps.append(jnp.dot(window.T, flat_grad, preferred_element_type=jnp.float32))
    local_grad = jnp.stack(taps).reshape(-1)
    summed = radix_sum(local_grad, ROUNDS)
    count = video.shape[0] * lax.axis_size(TM) * band_rows * lax.axis_size(SPACE) * band_cols
    return (conv_grad, summed * (1.0 / math.sqrt(count)))


def solution(mesh):
    tm_count, space_count = mesh.devices.shape
    grid = mesh.devices.reshape(tm_count // 16, 8, 2, space_count)
    fine = Mesh(grid, ("z", "y", "c", "x"))
    placed = (P(TM, SPACE, None, None), P(), P(), P(), P(), P(TM, SPACE, None, None))
    return jax.shard_map(
        per_device,
        mesh=fine,
        in_specs=placed,
        out_specs=(P(TM, SPACE, None, None), P(TM + (SPACE,))),
        check_vma=False,
    )
```

```python
import math

import jax
import jax.numpy as jnp
from jax import lax
from jax.sharding import Mesh, PartitionSpec as P

TM = ("z", "y", "c")
SPACE = "x"
ROUNDS = (("z", "y"), ("c", "x"))
AXES = ("z", "y", "c", "x")
MODE = 'a2a'


def swapped(value, axis, bit):
    mask = 2**bit
    pairs = [(source, source ^ mask) for source in range(lax.axis_size(axis))]
    return lax.ppermute(value, axis, pairs)


def with_halo(block, sides, width):
    for axis, dim in sides:
        count = lax.axis_size(axis)
        forward = [(i, i + 1) for i in range(count - 1)]
        backward = [(target, source) for source, target in forward]
        low = lax.ppermute(
            lax.slice_in_dim(block, block.shape[dim] - width, None, axis=dim), axis, forward
        )
        high = lax.ppermute(lax.slice_in_dim(block, 0, width, axis=dim), axis, backward)
        block = jnp.concatenate([low, block, high], axis=dim)
    return block


def shifted(value, axis, steps):
    count = lax.axis_size(axis)
    first, last = (max(0, -steps), min(count, count - steps))
    return lax.ppermute(value, axis, [(source, source + steps) for source in range(first, last)])


def project(values, weight):
    flat = values.reshape(-1, values.shape[-1])
    result = jnp.dot(flat, weight, preferred_element_type=jnp.float32)
    return result.reshape(values.shape[:-1] + (weight.shape[-1],))


def spatial_conv(padded, w_space, band_rows, band_cols):
    total = None
    for row_tap in range(3):
        for col_tap in range(3):
            window = padded[..., row_tap : row_tap + band_rows, col_tap : col_tap + band_cols, :]
            term = project(window, w_space[row_tap, col_tap])
            total = term if total is None else total + term
    return total.astype(jnp.bfloat16)


def halving_sum(local_grad):
    position = lax.axis_index(("tm", "space"))
    levels = lax.axis_size(("tm", "space")).bit_length() - 1
    holding = local_grad
    for bit in reversed(range(levels)):
        half_len = holding.shape[0] // 2
        lower = holding[:half_len]
        upper = holding[half_len:]
        upper_side = position >> bit & 1 == 1
        keeping = jnp.where(upper_side, upper, lower)
        sending = jnp.where(upper_side, lower, upper)
        holding = keeping + swapped(sending, ("tm", "space"), bit)
    return holding


def radix_sum(local_grad, rounds):
    outer, inner = rounds
    inner_count = lax.axis_size(inner)
    outer_count = lax.axis_size(outer)
    holding = local_grad.reshape(outer_count, inner_count, -1)
    holding = lax.all_to_all(holding.astype(jnp.bfloat16), inner, 1, 1, tiled=True)
    holding = holding.astype(jnp.float32).sum(axis=1)
    holding = lax.all_to_all(holding, outer, 0, 0, tiled=True).sum(axis=0)
    return holding

def per_device(video, w_space, w_time, w_merge1, w_merge2, cotangent):
    band_rows = video.shape[1]
    band_cols = video.shape[2]
    channels = video.shape[3]
    with_rows = with_halo(video, ((SPACE, 1),), 1)
    padded = jnp.pad(with_rows, ((0, 0), (0, 0), (1, 1), (0, 0)))
    conv = spatial_conv(padded, w_space, band_rows, band_cols)
    earlier = shifted(conv, TM, 1)
    history = jnp.concatenate([earlier, conv], axis=0)
    preact = (
        project(history[2:4], w_time[0])
        + project(history[1:3], w_time[1])
        + project(history[0:2], w_time[2])
    )
    parity = lax.axis_index(TM) % 2
    own_half = cotangent[0]
    level_weight = lax.dynamic_index_in_dim(w_merge2, parity, 0, keepdims=False)
    partner_half = swapped(cotangent, TM, 0)[0]
    leading = jnp.where(parity == 0, own_half, partner_half)
    trailing = jnp.where(parity == 0, partner_half, own_half)
    full_grad = jnp.concatenate([leading, trailing], axis=-1)
    level_sum = project(full_grad, level_weight.T)
    level_grad = level_sum.astype(jnp.bfloat16)
    hidden_grad = jnp.stack(
        [project(level_grad, w_merge1[0].T), project(level_grad, w_merge1[1].T)]
    )
    sigmoid_a = jax.nn.sigmoid(preact)
    slope = sigmoid_a * (1.0 + preact * (1.0 - sigmoid_a))
    act_grad = (hidden_grad * slope).astype(jnp.bfloat16)
    later = shifted(act_grad, TM, -1)
    future = jnp.concatenate([act_grad, later], axis=0)
    conv_sum = (
        project(future[0:2], w_time[0].T)
        + project(future[1:3], w_time[1].T)
        + project(future[2:4], w_time[2].T)
    )
    conv_grad = conv_sum.astype(jnp.bfloat16)
    flat_grad = conv_grad.reshape(-1, channels)
    taps = []
    for row_tap in range(3):
        for col_tap in range(3):
            window = padded[
                :, row_tap : row_tap + band_rows, col_tap : col_tap + band_cols, :
            ].reshape(-1, channels)
            taps.append(jnp.dot(window.T, flat_grad, preferred_element_type=jnp.float32))
    local_grad = jnp.stack(taps).reshape(-1)
    summed = radix_sum(local_grad, ROUNDS)
    count = video.shape[0] * lax.axis_size(TM) * band_rows * lax.axis_size(SPACE) * band_cols
    return (conv_grad, summed * (1.0 / math.sqrt(count)))


def solution(mesh):
    tm_count, space_count = mesh.devices.shape
    grid = mesh.devices.reshape(tm_count // 16, 8, 2, space_count)
    fine = Mesh(grid, ("z", "y", "c", "x"))
    placed = (P(TM, SPACE, None, None), P(), P(), P(), P(), P(TM, SPACE, None, None))
    return jax.shard_map(
        per_device,
        mesh=fine,
        in_specs=placed,
        out_specs=(P(TM, SPACE, None, None), P(TM + (SPACE,))),
        check_vma=False,
    )
```

```python
import math

import jax
import jax.numpy as jnp
from jax import lax
from jax.sharding import Mesh, PartitionSpec as P

TM = ("z", "y", "c")
SPACE = "x"
ROUNDS = (("z", "y"), ("c", "x"))
AXES = ("z", "y", "c", "x")
MODE = 'a2a'


def swapped(value, axis, bit):
    mask = 2**bit
    pairs = [(source, source ^ mask) for source in range(lax.axis_size(axis))]
    return lax.ppermute(value, axis, pairs)


def with_halo(block, sides, width):
    for axis, dim in sides:
        count = lax.axis_size(axis)
        forward = [(i, i + 1) for i in range(count - 1)]
        backward = [(target, source) for source, target in forward]
        low = lax.ppermute(
            lax.slice_in_dim(block, block.shape[dim] - width, None, axis=dim), axis, forward
        )
        high = lax.ppermute(lax.slice_in_dim(block, 0, width, axis=dim), axis, backward)
        block = jnp.concatenate([low, block, high], axis=dim)
    return block


def shifted(value, axis, steps):
    count = lax.axis_size(axis)
    first, last = (max(0, -steps), min(count, count - steps))
    return lax.ppermute(value, axis, [(source, source + steps) for source in range(first, last)])


def project(values, weight):
    flat = values.reshape(-1, values.shape[-1])
    result = jnp.dot(flat, weight, preferred_element_type=jnp.float32)
    return result.reshape(values.shape[:-1] + (weight.shape[-1],))


def spatial_conv(padded, w_space, band_rows, band_cols):
    total = None
    for row_tap in range(3):
        for col_tap in range(3):
            window = padded[..., row_tap : row_tap + band_rows, col_tap : col_tap + band_cols, :]
            term = project(window, w_space[row_tap, col_tap])
            total = term if total is None else total + term
    return total.astype(jnp.bfloat16)


def halving_sum(local_grad):
    position = lax.axis_index(("tm", "space"))
    levels = lax.axis_size(("tm", "space")).bit_length() - 1
    holding = local_grad
    for bit in reversed(range(levels)):
        half_len = holding.shape[0] // 2
        lower = holding[:half_len]
        upper = holding[half_len:]
        upper_side = position >> bit & 1 == 1
        keeping = jnp.where(upper_side, upper, lower)
        sending = jnp.where(upper_side, lower, upper)
        holding = keeping + swapped(sending, ("tm", "space"), bit)
    return holding


def radix_sum(local_grad, rounds, scale):
    outer, inner = rounds
    inner_count = lax.axis_size(inner)
    outer_count = lax.axis_size(outer)
    holding = local_grad.reshape(outer_count, inner_count, -1)
    holding = lax.all_to_all(holding, inner, 1, 1, tiled=True)
    holding = holding.astype(jnp.float32).sum(axis=1) * scale
    holding = lax.all_to_all(holding, outer, 0, 0, tiled=True).sum(axis=0)
    return holding

def per_device(video, w_space, w_time, w_merge1, w_merge2, cotangent):
    band_rows = video.shape[1]
    band_cols = video.shape[2]
    channels = video.shape[3]
    with_rows = with_halo(video, ((SPACE, 1),), 1)
    padded = jnp.pad(with_rows, ((0, 0), (0, 0), (1, 1), (0, 0)))
    conv = spatial_conv(padded, w_space, band_rows, band_cols)
    earlier = shifted(conv, TM, 1)
    history = jnp.concatenate([earlier, conv], axis=0)
    preact = (
        project(history[2:4], w_time[0])
        + project(history[1:3], w_time[1])
        + project(history[0:2], w_time[2])
    )
    parity = lax.axis_index(TM) % 2
    own_half = cotangent[0]
    level_weight = lax.dynamic_index_in_dim(w_merge2, parity, 0, keepdims=False)
    partner_half = swapped(cotangent, TM, 0)[0]
    leading = jnp.where(parity == 0, own_half, partner_half)
    trailing = jnp.where(parity == 0, partner_half, own_half)
    full_grad = jnp.concatenate([leading, trailing], axis=-1)
    level_sum = project(full_grad, level_weight.T)
    level_grad = level_sum.astype(jnp.bfloat16)
    hidden_grad = jnp.stack(
        [project(level_grad, w_merge1[0].T), project(level_grad, w_merge1[1].T)]
    )
    sigmoid_a = jax.nn.sigmoid(preact)
    slope = sigmoid_a * (1.0 + preact * (1.0 - sigmoid_a))
    act_grad = (hidden_grad * slope).astype(jnp.bfloat16)
    later = shifted(act_grad, TM, -1)
    future = jnp.concatenate([act_grad, later], axis=0)
    conv_sum = (
        project(future[0:2], w_time[0].T)
        + project(future[1:3], w_time[1].T)
        + project(future[2:4], w_time[2].T)
    )
    conv_grad = conv_sum.astype(jnp.bfloat16)
    flat_grad = conv_grad.reshape(-1, channels)
    taps = []
    for row_tap in range(3):
        for col_tap in range(3):
            window = padded[
                :, row_tap : row_tap + band_rows, col_tap : col_tap + band_cols, :
            ].reshape(-1, channels)
            taps.append(
                jnp.dot(window.T, flat_grad, preferred_element_type=jnp.float32).astype(jnp.bfloat16)
            )
    local_grad = jnp.stack(taps).reshape(-1)
    count = video.shape[0] * lax.axis_size(TM) * band_rows * lax.axis_size(SPACE) * band_cols
    summed = radix_sum(local_grad, ROUNDS, 1.0 / math.sqrt(count))
    return (conv_grad, summed)


def solution(mesh):
    tm_count, space_count = mesh.devices.shape
    grid = mesh.devices.reshape(tm_count // 16, 8, 2, space_count)
    fine = Mesh(grid, ("z", "y", "c", "x"))
    placed = (P(TM, SPACE, None, None), P(), P(), P(), P(), P(TM, SPACE, None, None))
    return jax.shard_map(
        per_device,
        mesh=fine,
        in_specs=placed,
        out_specs=(P(TM, SPACE, None, None), P(TM + (SPACE,))),
        check_vma=False,
    )
```

```python
import math

import jax
import jax.numpy as jnp
from jax import lax
from jax.sharding import Mesh, PartitionSpec as P

TM = ("z", "y", "c")
SPACE = "x"
ROUNDS = (("z", "y"), ("c", "x"))
AXES = ("z", "y", "c", "x")
MODE = 'a2a'


def swapped(value, axis, bit):
    mask = 2**bit
    pairs = [(source, source ^ mask) for source in range(lax.axis_size(axis))]
    return lax.ppermute(value, axis, pairs)


def with_halo(block, sides, width):
    for axis, dim in sides:
        count = lax.axis_size(axis)
        forward = [(i, i + 1) for i in range(count - 1)]
        backward = [(target, source) for source, target in forward]
        low = lax.ppermute(
            lax.slice_in_dim(block, block.shape[dim] - width, None, axis=dim), axis, forward
        )
        high = lax.ppermute(lax.slice_in_dim(block, 0, width, axis=dim), axis, backward)
        block = jnp.concatenate([low, block, high], axis=dim)
    return block


def shifted(value, axis, steps):
    count = lax.axis_size(axis)
    first, last = (max(0, -steps), min(count, count - steps))
    return lax.ppermute(value, axis, [(source, source + steps) for source in range(first, last)])


def project(values, weight):
    flat = values.reshape(-1, values.shape[-1])
    result = jnp.dot(flat, weight, preferred_element_type=jnp.float32)
    return result.reshape(values.shape[:-1] + (weight.shape[-1],))


def spatial_conv(padded, w_space, band_rows, band_cols):
    total = lax.conv_general_dilated(
        padded, w_space, (1, 1), "VALID",
        dimension_numbers=("NHWC", "HWIO", "NHWC"),
        preferred_element_type=jnp.float32,
    )
    return total.astype(jnp.bfloat16)

def halving_sum(local_grad):
    position = lax.axis_index(("tm", "space"))
    levels = lax.axis_size(("tm", "space")).bit_length() - 1
    holding = local_grad
    for bit in reversed(range(levels)):
        half_len = holding.shape[0] // 2
        lower = holding[:half_len]
        upper = holding[half_len:]
        upper_side = position >> bit & 1 == 1
        keeping = jnp.where(upper_side, upper, lower)
        sending = jnp.where(upper_side, lower, upper)
        holding = keeping + swapped(sending, ("tm", "space"), bit)
    return holding


def radix_sum(local_grad, rounds, scale):
    outer, inner = rounds
    inner_count = lax.axis_size(inner)
    outer_count = lax.axis_size(outer)
    holding = local_grad.reshape(outer_count, inner_count, -1)
    holding = lax.all_to_all(holding, inner, 1, 1, tiled=True)
    holding = holding.astype(jnp.float32).sum(axis=1) * scale
    holding = lax.all_to_all(holding, outer, 0, 0, tiled=True).sum(axis=0)
    return holding

def per_device(video, w_space, w_time, w_merge1, w_merge2, cotangent):
    band_rows = video.shape[1]
    band_cols = video.shape[2]
    channels = video.shape[3]
    with_rows = with_halo(video, ((SPACE, 1),), 1)
    padded = jnp.pad(with_rows, ((0, 0), (0, 0), (1, 1), (0, 0)))
    conv = spatial_conv(padded, w_space, band_rows, band_cols)
    earlier = shifted(conv, TM, 1)
    history = jnp.concatenate([earlier, conv], axis=0)
    preact = (
        project(history[2:4], w_time[0])
        + project(history[1:3], w_time[1])
        + project(history[0:2], w_time[2])
    )
    parity = lax.axis_index(TM) % 2
    own_half = cotangent[0]
    level_weight = lax.dynamic_index_in_dim(w_merge2, parity, 0, keepdims=False)
    partner_half = swapped(cotangent, TM, 0)[0]
    leading = jnp.where(parity == 0, own_half, partner_half)
    trailing = jnp.where(parity == 0, partner_half, own_half)
    full_grad = jnp.concatenate([leading, trailing], axis=-1)
    level_sum = project(full_grad, level_weight.T)
    level_grad = level_sum.astype(jnp.bfloat16)
    hidden_grad = jnp.stack(
        [project(level_grad, w_merge1[0].T), project(level_grad, w_merge1[1].T)]
    )
    sigmoid_a = jax.nn.sigmoid(preact)
    slope = sigmoid_a * (1.0 + preact * (1.0 - sigmoid_a))
    act_grad = (hidden_grad * slope).astype(jnp.bfloat16)
    later = shifted(act_grad, TM, -1)
    future = jnp.concatenate([act_grad, later], axis=0)
    conv_sum = (
        project(future[0:2], w_time[0].T)
        + project(future[1:3], w_time[1].T)
        + project(future[2:4], w_time[2].T)
    )
    conv_grad = conv_sum.astype(jnp.bfloat16)
    flat_grad = conv_grad.reshape(-1, channels)
    taps = []
    for row_tap in range(3):
        for col_tap in range(3):
            window = padded[
                :, row_tap : row_tap + band_rows, col_tap : col_tap + band_cols, :
            ].reshape(-1, channels)
            taps.append(
                jnp.dot(window.T, flat_grad, preferred_element_type=jnp.float32).astype(jnp.bfloat16)
            )
    local_grad = jnp.stack(taps).reshape(-1)
    count = video.shape[0] * lax.axis_size(TM) * band_rows * lax.axis_size(SPACE) * band_cols
    summed = radix_sum(local_grad, ROUNDS, 1.0 / math.sqrt(count))
    return (conv_grad, summed)


def solution(mesh):
    tm_count, space_count = mesh.devices.shape
    grid = mesh.devices.reshape(tm_count // 16, 8, 2, space_count)
    fine = Mesh(grid, ("z", "y", "c", "x"))
    placed = (P(TM, SPACE, None, None), P(), P(), P(), P(), P(TM, SPACE, None, None))
    return jax.shard_map(
        per_device,
        mesh=fine,
        in_specs=placed,
        out_specs=(P(TM, SPACE, None, None), P(TM + (SPACE,))),
        check_vma=False,
    )
```

```python
import math

import jax
import jax.numpy as jnp
from jax import lax
from jax.sharding import Mesh, PartitionSpec as P

TM = ("z", "y", "c")
SPACE = "x"
ROUNDS = (("z", "y"), ("c", "x"))
AXES = ("z", "y", "c", "x")
MODE = 'a2a'


def swapped(value, axis, bit):
    mask = 2**bit
    pairs = [(source, source ^ mask) for source in range(lax.axis_size(axis))]
    return lax.ppermute(value, axis, pairs)


def with_halo(block, sides, width):
    for axis, dim in sides:
        count = lax.axis_size(axis)
        forward = [(i, i + 1) for i in range(count - 1)]
        backward = [(target, source) for source, target in forward]
        low = lax.ppermute(
            lax.slice_in_dim(block, block.shape[dim] - width, None, axis=dim), axis, forward
        )
        high = lax.ppermute(lax.slice_in_dim(block, 0, width, axis=dim), axis, backward)
        block = jnp.concatenate([low, block, high], axis=dim)
    return block


def shifted(value, axis, steps):
    count = lax.axis_size(axis)
    first, last = (max(0, -steps), min(count, count - steps))
    return lax.ppermute(value, axis, [(source, source + steps) for source in range(first, last)])


def project(values, weight):
    flat = values.reshape(-1, values.shape[-1])
    result = jnp.dot(flat, weight, preferred_element_type=jnp.float32)
    return result.reshape(values.shape[:-1] + (weight.shape[-1],))


def spatial_conv(padded, w_space, band_rows, band_cols):
    total = None
    for row_tap in range(3):
        for col_tap in range(3):
            window = padded[..., row_tap : row_tap + band_rows, col_tap : col_tap + band_cols, :]
            term = project(window, w_space[row_tap, col_tap])
            total = term if total is None else total + term
    return total.astype(jnp.bfloat16)


def halving_sum(local_grad):
    position = lax.axis_index(("tm", "space"))
    levels = lax.axis_size(("tm", "space")).bit_length() - 1
    holding = local_grad
    for bit in reversed(range(levels)):
        half_len = holding.shape[0] // 2
        lower = holding[:half_len]
        upper = holding[half_len:]
        upper_side = position >> bit & 1 == 1
        keeping = jnp.where(upper_side, upper, lower)
        sending = jnp.where(upper_side, lower, upper)
        holding = keeping + swapped(sending, ("tm", "space"), bit)
    return holding


def radix_sum(local_grad, rounds, scale):
    outer, inner = rounds
    inner_count = lax.axis_size(inner)
    outer_count = lax.axis_size(outer)
    holding = local_grad.reshape(outer_count, inner_count, -1)
    holding = lax.all_to_all(holding, inner, 1, 1, tiled=True)
    holding = holding.astype(jnp.float32).sum(axis=1) * scale
    holding = lax.all_to_all(holding.astype(jnp.bfloat16), outer, 0, 0, tiled=True)
    holding = holding.astype(jnp.float32).sum(axis=0)
    return holding

def per_device(video, w_space, w_time, w_merge1, w_merge2, cotangent):
    band_rows = video.shape[1]
    band_cols = video.shape[2]
    channels = video.shape[3]
    with_rows = with_halo(video, ((SPACE, 1),), 1)
    padded = jnp.pad(with_rows, ((0, 0), (0, 0), (1, 1), (0, 0)))
    conv = spatial_conv(padded, w_space, band_rows, band_cols)
    earlier = shifted(conv, TM, 1)
    history = jnp.concatenate([earlier, conv], axis=0)
    preact = (
        project(history[2:4], w_time[0])
        + project(history[1:3], w_time[1])
        + project(history[0:2], w_time[2])
    )
    parity = lax.axis_index(TM) % 2
    own_half = cotangent[0]
    level_weight = lax.dynamic_index_in_dim(w_merge2, parity, 0, keepdims=False)
    partner_half = swapped(cotangent, TM, 0)[0]
    leading = jnp.where(parity == 0, own_half, partner_half)
    trailing = jnp.where(parity == 0, partner_half, own_half)
    full_grad = jnp.concatenate([leading, trailing], axis=-1)
    level_sum = project(full_grad, level_weight.T)
    level_grad = level_sum.astype(jnp.bfloat16)
    hidden_grad = jnp.stack(
        [project(level_grad, w_merge1[0].T), project(level_grad, w_merge1[1].T)]
    )
    sigmoid_a = jax.nn.sigmoid(preact)
    slope = sigmoid_a * (1.0 + preact * (1.0 - sigmoid_a))
    act_grad = (hidden_grad * slope).astype(jnp.bfloat16)
    later = shifted(act_grad, TM, -1)
    future = jnp.concatenate([act_grad, later], axis=0)
    conv_sum = (
        project(future[0:2], w_time[0].T)
        + project(future[1:3], w_time[1].T)
        + project(future[2:4], w_time[2].T)
    )
    conv_grad = conv_sum.astype(jnp.bfloat16)
    flat_grad = conv_grad.reshape(-1, channels)
    taps = []
    for row_tap in range(3):
        for col_tap in range(3):
            window = padded[
                :, row_tap : row_tap + band_rows, col_tap : col_tap + band_cols, :
            ].reshape(-1, channels)
            taps.append(
                jnp.dot(window.T, flat_grad, preferred_element_type=jnp.float32).astype(jnp.bfloat16)
            )
    local_grad = jnp.stack(taps).reshape(-1)
    count = video.shape[0] * lax.axis_size(TM) * band_rows * lax.axis_size(SPACE) * band_cols
    summed = radix_sum(local_grad, ROUNDS, 1.0 / math.sqrt(count))
    return (conv_grad, summed)


def solution(mesh):
    tm_count, space_count = mesh.devices.shape
    grid = mesh.devices.reshape(tm_count // 16, 8, 2, space_count)
    fine = Mesh(grid, ("z", "y", "c", "x"))
    placed = (P(TM, SPACE, None, None), P(), P(), P(), P(), P(TM, SPACE, None, None))
    return jax.shard_map(
        per_device,
        mesh=fine,
        in_specs=placed,
        out_specs=(P(TM, SPACE, None, None), P(TM + (SPACE,))),
        check_vma=False,
    )
```

```python
import math

import jax
import jax.numpy as jnp
from jax import lax
from jax.sharding import Mesh, PartitionSpec as P

TM = ("z", "y", "c")
SPACE = "x"
ROUNDS = (("z", "y"), ("c", "x"))
AXES = ("z", "y", "c", "x")
MODE = 'a2a'


def swapped(value, axis, bit):
    mask = 2**bit
    pairs = [(source, source ^ mask) for source in range(lax.axis_size(axis))]
    return lax.ppermute(value, axis, pairs)


def with_halo(block, sides, width):
    for axis, dim in sides:
        count = lax.axis_size(axis)
        forward = [(i, i + 1) for i in range(count - 1)]
        backward = [(target, source) for source, target in forward]
        low = lax.ppermute(
            lax.slice_in_dim(block, block.shape[dim] - width, None, axis=dim), axis, forward
        )
        high = lax.ppermute(lax.slice_in_dim(block, 0, width, axis=dim), axis, backward)
        block = jnp.concatenate([low, block, high], axis=dim)
    return block


def shifted(value, axis, steps):
    count = lax.axis_size(axis)
    first, last = (max(0, -steps), min(count, count - steps))
    return lax.ppermute(value, axis, [(source, source + steps) for source in range(first, last)])


def project(values, weight):
    flat = values.reshape(-1, values.shape[-1])
    result = jnp.dot(flat, weight, preferred_element_type=jnp.float32)
    return result.reshape(values.shape[:-1] + (weight.shape[-1],))


def spatial_conv(padded, w_space, band_rows, band_cols):
    total = None
    for row_tap in range(3):
        for col_tap in range(3):
            window = padded[..., row_tap : row_tap + band_rows, col_tap : col_tap + band_cols, :]
            term = project(window, w_space[row_tap, col_tap])
            total = term if total is None else total + term
    return total.astype(jnp.bfloat16)


def halving_sum(local_grad):
    position = lax.axis_index(("tm", "space"))
    levels = lax.axis_size(("tm", "space")).bit_length() - 1
    holding = local_grad
    for bit in reversed(range(levels)):
        half_len = holding.shape[0] // 2
        lower = holding[:half_len]
        upper = holding[half_len:]
        upper_side = position >> bit & 1 == 1
        keeping = jnp.where(upper_side, upper, lower)
        sending = jnp.where(upper_side, lower, upper)
        holding = keeping + swapped(sending, ("tm", "space"), bit)
    return holding


def radix_sum(local_grad, rounds, scale):
    outer, inner = rounds
    inner_count = lax.axis_size(inner)
    outer_count = lax.axis_size(outer)
    holding = local_grad.reshape(outer_count, lax.axis_size(inner[0]), lax.axis_size(inner[1]), -1)
    holding = holding.transpose(0, 2, 1, 3).reshape(outer_count, inner_count, -1)
    inner = (inner[1], inner[0])
    holding = lax.all_to_all(holding, inner, 1, 1, tiled=True)
    holding = holding.astype(jnp.float32).sum(axis=1) * scale
    holding = lax.all_to_all(holding, outer, 0, 0, tiled=True).sum(axis=0)
    return holding

def per_device(video, w_space, w_time, w_merge1, w_merge2, cotangent):
    band_rows = video.shape[1]
    band_cols = video.shape[2]
    channels = video.shape[3]
    with_rows = with_halo(video, ((SPACE, 1),), 1)
    padded = jnp.pad(with_rows, ((0, 0), (0, 0), (1, 1), (0, 0)))
    conv = spatial_conv(padded, w_space, band_rows, band_cols)
    earlier = shifted(conv, TM, 1)
    history = jnp.concatenate([earlier, conv], axis=0)
    preact = (
        project(history[2:4], w_time[0])
        + project(history[1:3], w_time[1])
        + project(history[0:2], w_time[2])
    )
    parity = lax.axis_index(TM) % 2
    own_half = cotangent[0]
    level_weight = lax.dynamic_index_in_dim(w_merge2, parity, 0, keepdims=False)
    partner_half = swapped(cotangent, TM, 0)[0]
    leading = jnp.where(parity == 0, own_half, partner_half)
    trailing = jnp.where(parity == 0, partner_half, own_half)
    full_grad = jnp.concatenate([leading, trailing], axis=-1)
    level_sum = project(full_grad, level_weight.T)
    level_grad = level_sum.astype(jnp.bfloat16)
    hidden_grad = jnp.stack(
        [project(level_grad, w_merge1[0].T), project(level_grad, w_merge1[1].T)]
    )
    sigmoid_a = jax.nn.sigmoid(preact)
    slope = sigmoid_a * (1.0 + preact * (1.0 - sigmoid_a))
    act_grad = (hidden_grad * slope).astype(jnp.bfloat16)
    later = shifted(act_grad, TM, -1)
    future = jnp.concatenate([act_grad, later], axis=0)
    conv_sum = (
        project(future[0:2], w_time[0].T)
        + project(future[1:3], w_time[1].T)
        + project(future[2:4], w_time[2].T)
    )
    conv_grad = conv_sum.astype(jnp.bfloat16)
    flat_grad = conv_grad.reshape(-1, channels)
    taps = []
    for row_tap in range(3):
        for col_tap in range(3):
            window = padded[
                :, row_tap : row_tap + band_rows, col_tap : col_tap + band_cols, :
            ].reshape(-1, channels)
            taps.append(
                jnp.dot(window.T, flat_grad, preferred_element_type=jnp.float32).astype(jnp.bfloat16)
            )
    local_grad = jnp.stack(taps).reshape(-1)
    count = video.shape[0] * lax.axis_size(TM) * band_rows * lax.axis_size(SPACE) * band_cols
    summed = radix_sum(local_grad, ROUNDS, 1.0 / math.sqrt(count))
    return (conv_grad, summed)


def solution(mesh):
    tm_count, space_count = mesh.devices.shape
    grid = mesh.devices.reshape(tm_count // 16, 8, 2, space_count)
    fine = Mesh(grid, ("z", "y", "c", "x"))
    placed = (P(TM, SPACE, None, None), P(), P(), P(), P(), P(TM, SPACE, None, None))
    return jax.shard_map(
        per_device,
        mesh=fine,
        in_specs=placed,
        out_specs=(P(TM, SPACE, None, None), P(TM + (SPACE,))),
        check_vma=False,
    )
```
